256 devices in a mesh: cfg: 2 (over x_hi), gx: 8 (over y, x_lo), gy: 16 (over z, core).
Axes of the slice: x: 4 (x_hi: 2, x_lo: 2; x = x_hi * 2 + x_lo), y: 4, z: 8, core: 2. Of those that a mesh axis runs over, the one named last changes fastest.
Arguments:
- descriptors: bfloat16 [2, 8, 32, 64, 128], P('cfg', 'gx', 'gy'), may hold values from -0.5 to 0.5
- derivatives: bfloat16 [2, 8, 32, 64, 16, 3, 128], P('cfg', 'gx', 'gy'), may hold values from -6 to 6
- neighbours: int32 [2, 8, 32, 64, 16], P('cfg', 'gx', 'gy'), may hold values from 0 to 575
- valid: int32 [2, 8, 32, 64], P('cfg', 'gx', 'gy'), may hold values from 0 to 1, as said below
- forces: bfloat16 [2, 8, 32, 64, 3], P('cfg', 'gx', 'gy'), may hold values from -6 to 6
- pool: bfloat16 [2048, 128], replicated, may hold values from -0.5 to 0.5
- sparse_idx: int32 [1024], replicated, may hold values from 0 to 2047, as said below
Outputs:
- design: bfloat16 [2, 8, 32, 64, 3, 1024], P('cfg', 'gx', 'gy')
- gram: float32 [1024, 1024], P(('gx', 'gy'))
- rhs: float32 [1024], P(('gx', 'gy'))
The draws below stay inside these ranges and needn't reach their ends.
Inputs may be any that keep to these rules, and one draw needn't show every extreme that they name: `valid`: the first atom of every tile is real. `sparse_idx`: distinct rows.
All inputs are finite; a program needn't handle non-finite values.
Results may differ from the reference program's by a relative error of at most 0.0031.
Values sent between devices are 32-bit elements; how exact they have to be, the bound alone decides.
No kernel may reach another device: no remote copies, remote signals or barrier semaphores. Data moves between devices by JAX's collectives and lax.ppermute only.
A program may use at most 128 MiB of HBM per device.

```python
import jax
import jax.numpy as jnp
from jax import lax

DESC = 128
M = 1024
POOL = 2048
K = 16
CFG = 2
NTX = 8
NTY = 32


def draw_valid(key, part):
    levels = jax.random.randint(key, (CFG, NTX, NTY, 64), 0, 5)
    marks = (levels > 0).astype(jnp.int32)
    return marks.at[:, :, :, 0].set(1)


def draw_sparse_idx(key, part):
    order = jax.random.permutation(key, POOL)
    return order[:M].astype(jnp.int32)


def place_ends(drawn, stream_key, least, largest):
    spot = [jax.random.randint(jax.random.fold_in(stream_key, axis), (), 0, length) for axis, length in enumerate(drawn.shape)]
    longest = drawn.shape.index(max(drawn.shape))
    beside = spot[:longest] + [(spot[longest] + 1) % drawn.shape[longest]] + spot[longest + 1:]
    return drawn.at[tuple(spot)].set(least).at[tuple(beside)].set(largest)


def block_levels(stream_key, extent, pieces, smallest, high):
    gain, own = 1.0, jax.random.fold_in(stream_key, 6)
    for dim, shards_of in pieces:
        heights = jnp.exp(jax.random.uniform(jax.random.fold_in(own, dim), (shards_of,), jnp.float32, smallest / len(pieces), high / len(pieces)))
        gain = gain * jnp.repeat(heights, extent[dim] // shards_of).reshape([-1 if axis == dim else 1 for axis in range(len(extent))])
    return gain


def scatter_about(own_key, extent, spread, limit, split=(), kind=jnp.bfloat16):
    array = jax.random.normal(own_key, extent, jnp.float32) * spread
    if len(split) > 0:
        array = block_levels(own_key, extent, split, -0.22, 0.18) * array
    return jnp.clip(array, min=-limit, max=limit).astype(kind)


def setup_inputs(seed: int = 0) -> dict:
    splits = jax.random.split(jax.random.key(seed), 8)
    return {
        "descriptors": scatter_about(splits[0], (CFG, NTX, NTY, 64, DESC), DESC ** -0.5, 0.5, ((0, 2), (1, 8), (2, 16))),
        "derivatives": scatter_about(splits[1], (CFG, NTX, NTY, 64, K, 3, DESC), 1.0, 6.0, ((0, 2), (1, 8), (2, 16))),
        "neighbours": place_ends(jax.random.randint(splits[2], (CFG, NTX, NTY, 64, K), 0, 576), jax.random.fold_in(splits[2], 1), 0, 575).astype(jnp.int32),
        "valid": draw_valid(jax.random.fold_in(splits[7], 71), 0),
        "forces": scatter_about(splits[4], (CFG, NTX, NTY, 64, 3), 1.0, 6.0, ((0, 2), (1, 8), (2, 16))),
        "pool": scatter_about(splits[5], (POOL, DESC), DESC ** -0.5, 0.5),
        "sparse_idx": draw_sparse_idx(jax.random.fold_in(splits[7], 71), 0),
    }


def reference(descriptors, derivatives, neighbours, valid, forces, pool, sparse_idx):
    sparse = pool[sparse_idx]
    groups = descriptors.shape[0]
    tiles_x = descriptors.shape[1]
    tiles_y = descriptors.shape[2]
    total_tiles = groups * tiles_x * tiles_y
    flat_desc = descriptors.reshape(total_tiles, 64, DESC)
    flat_deriv = derivatives.reshape(total_tiles, 64 * K * 3, DESC)
    flat_nbr = neighbours.reshape(total_tiles, 64, K)
    flat_valid = valid.reshape(total_tiles, 64)
    tile_ids = jnp.arange(total_tiles, dtype=jnp.int32)
    accumulator = jnp.zeros((total_tiles * 64, 3, M), jnp.float32)

    def add_tile(accumulator, inputs):
        tile_id, desc_tile, deriv_tile, nbr_tile, valid_tile = inputs
        group_id = tile_id // (tiles_x * tiles_y)
        remain = tile_id % (tiles_x * tiles_y)
        tile_x = remain // tiles_y
        tile_y = remain % tiles_y
        scores = jnp.dot(desc_tile, sparse.T, preferred_element_type=jnp.float32)
        scores = scores * valid_tile[:, None].astype(jnp.float32)
        projected = jnp.dot(deriv_tile, sparse.T, preferred_element_type=jnp.float32).reshape(64, K, 3, M)
        contribution = -2.0 * scores[:, None, None, :] * projected
        slot_code = nbr_tile // 64
        target_atom = nbr_tile % 64
        target_x = (tile_x + slot_code // 3 - 1 + tiles_x) % tiles_x
        target_y = (tile_y + slot_code % 3 - 1 + tiles_y) % tiles_y
        target = ((group_id * tiles_x + target_x) * tiles_y + target_y) * 64 + target_atom
        accumulator = accumulator.at[target.reshape(-1).astype(jnp.int32)].add(contribution.reshape(64 * K, 3, M))
        return accumulator, None

    accumulator, _ = lax.scan(add_tile, accumulator, (tile_ids, flat_desc, flat_deriv, flat_nbr, flat_valid))
    design = accumulator.astype(jnp.bfloat16).reshape(groups, tiles_x, tiles_y, 64, 3, M)
    gram = jnp.zeros((M, M), jnp.float32)
    rhs = jnp.zeros((M,), jnp.float32)
    for group_id in range(groups):
        valid_group = valid[group_id]
        masked = design[group_id] * valid_group[:, :, :, None, None].astype(jnp.bfloat16)
        masked_rows = masked.reshape(-1, M)
        force_group = forces[group_id].astype(jnp.float32)
        sumsq = jnp.sum(valid_group[:, :, :, None].astype(jnp.float32) * force_group * force_group)
        gram_part = lax.dot_general(masked_rows, masked_rows, (((0,), (0,)), ((), ())), preferred_element_type=jnp.float32)
        rhs_part = jnp.dot(forces[group_id].reshape(-1), masked_rows, preferred_element_type=jnp.float32)
        gram = gram + gram_part / sumsq
        rhs = rhs + rhs_part / sumsq
    return design, gram, rhs
```

```python
import jax
import jax.numpy as jnp
from jax import lax
from jax.sharding import PartitionSpec as P


def passed_along(x, axis, by):
    length = lax.axis_size(axis)
    return lax.ppermute(x, axis, [(i, (i + by) % length) for i in range(length)])


def fold_x(slab_array):
    inner_count = slab_array.shape[0] - 2
    from_high = passed_along(slab_array[0], "gx", -1)
    from_low = passed_along(slab_array[inner_count + 1], "gx", 1)
    interior = slab_array[1 : inner_count + 1]
    interior = interior.at[inner_count - 1].add(from_high)
    interior = interior.at[0].add(from_low)
    return interior


def fold_y(slab_array):
    inner_count = slab_array.shape[1] - 2
    from_high = passed_along(slab_array[:, 0], "gy", -1)
    from_low = passed_along(slab_array[:, inner_count + 1], "gy", 1)
    interior = slab_array[:, 1 : inner_count + 1]
    interior = interior.at[:, inner_count - 1].add(from_high)
    interior = interior.at[:, 0].add(from_low)
    return interior


def halving_scatter(block, axis):
    length = lax.axis_size(axis)
    index = lax.axis_index(axis)
    distance = length // 2
    while distance >= 1:
        half = block.shape[0] // 2
        lower, upper = block[:half], block[half:]
        upper_side = (index // distance) % 2 == 1
        keep = jnp.where(upper_side, upper, lower)
        send = jnp.where(upper_side, lower, upper)
        pairs = [(i, i ^ distance) for i in range(length)]
        block = keep + lax.ppermute(send, axis, pairs)
        distance //= 2
    return block


def swapped(x, axis):
    length = lax.axis_size(axis)
    return lax.ppermute(x, axis, [(i, i ^ 1) for i in range(length)])


def per_device(descriptors, derivatives, neighbours, valid, forces, pool, sparse_idx):
    tiles_x = descriptors.shape[1]
    tiles_y = descriptors.shape[2]
    tile_count = tiles_x * tiles_y
    slot_total = derivatives.shape[4]
    desc_width = descriptors.shape[4]
    sparse = pool[sparse_idx]
    sparse_count = sparse.shape[0]
    rows = 64 * slot_total
    ext_rows = (tiles_x + 2) * (tiles_y + 2) * 64

    flat_valid = valid.reshape(tile_count, 64)
    flat_desc = descriptors.reshape(tile_count, 64, desc_width)
    flat_desc = jnp.where(flat_valid[:, :, None] != 0, flat_desc, jnp.zeros_like(flat_desc))
    scores = lax.dot_general(
        flat_desc, sparse, (((2,), (1,)), ((), ())), preferred_element_type=jnp.float32
    )
    flat_deriv = derivatives.reshape(tile_count, rows, 3, desc_width)
    projected = lax.dot_general(
        flat_deriv, sparse, (((3,), (1,)), ((), ())), preferred_element_type=jnp.float32
    )
    scores_rep = jnp.repeat(scores, slot_total, axis=1)
    contribution = (-2.0 * scores_rep)[:, :, None, :] * projected
    high_wide = lax.reduce_precision(contribution, exponent_bits=8, mantissa_bits=7)
    high = high_wide.astype(jnp.bfloat16)
    low = (contribution - high_wide).astype(jnp.bfloat16)
    parts = jnp.concatenate([high, low], axis=0).reshape(2 * tile_count, rows, 3 * sparse_count)

    tile_ids = jnp.arange(tile_count, dtype=jnp.int32)
    tile_x = (tile_ids // tiles_y)[:, None]
    tile_y = (tile_ids % tiles_y)[:, None]
    flat_nbr = neighbours.reshape(tile_count, rows)
    slot_code = flat_nbr // 64
    target_atom = flat_nbr % 64
    ext_x = tile_x + slot_code // 3
    ext_y = tile_y + slot_code % 3
    target = (ext_x * (tiles_y + 2) + ext_y) * 64 + target_atom
    onehot = (
        jnp.arange(ext_rows, dtype=jnp.int32)[None, :, None] == target[:, None, :]
    ).astype(jnp.bfloat16)
    onehot = jnp.concatenate([onehot, onehot], axis=0)
    accumulator = lax.dot_general(
        onehot, parts, (((0, 2), (0, 1)), ((), ())), preferred_element_type=jnp.float32
    )
    extended = accumulator.reshape(tiles_x + 2, tiles_y + 2, 64, 3, sparse_count)
    owned = fold_x(fold_y(extended))
    design = owned.astype(jnp.bfloat16)

    valid_own = valid[0]
    masked = design * valid_own[:, :, :, None, None].astype(jnp.bfloat16)
    masked_rows = masked.reshape(-1, sparse_count)
    force_own = forces[0].astype(jnp.float32)
    local_sumsq = jnp.sum(valid_own[:, :, :, None].astype(jnp.float32) * force_own * force_own)
    gram_part = lax.dot_general(
        masked_rows, masked_rows, (((0,), (0,)), ((), ())), preferred_element_type=jnp.float32
    )
    rhs_part = jnp.dot(forces[0].reshape(-1), masked_rows, preferred_element_type=jnp.float32)

    pad_cols = 128
    extra = jnp.zeros((sparse_count, pad_cols), jnp.float32)
    extra = extra.at[:, 0].set(rhs_part).at[:, 1].set(local_sumsq)
    packed = jnp.concatenate([gram_part, extra], axis=1)
    gx_size = lax.axis_size("gx")
    gy_size = lax.axis_size("gy")
    packed = packed.reshape(gx_size, gy_size, -1, packed.shape[1]).swapaxes(0, 1)
    packed = packed.reshape(sparse_count, -1)
    reduced = lax.psum_scatter(packed, "gy", scatter_dimension=0, tiled=True)
    reduced = halving_scatter(reduced, "gx")
    weighted = reduced / reduced[:, sparse_count + 1 : sparse_count + 2]
    total = weighted + swapped(weighted, "cfg")
    gram = total[:, :sparse_count]
    rhs = total[:, sparse_count]
    return (design[None], gram, rhs)


def solution(mesh):
    in_specs = (
        P("cfg", "gx", "gy", None, None),
        P("cfg", "gx", "gy", None, None, None, None),
        P("cfg", "gx", "gy", None, None),
        P("cfg", "gx", "gy", None),
        P("cfg", "gx", "gy", None, None),
        P(),
        P(),
    )
    out_specs = (P("cfg", "gx", "gy", None, None, None), P(("gx", "gy"), None), P(("gx", "gy")))
    return jax.shard_map(
        per_device, mesh=mesh, in_specs=in_specs, out_specs=out_specs, check_vma=False
    )
```

```python
import jax
import numpy as np
import jax.numpy as jnp
from jax import lax
from jax.sharding import PartitionSpec as P


def passed_along(x, axis, by):
    length = lax.axis_size(axis)
    return lax.ppermute(x, axis, [(i, (i + by) % length) for i in range(length)])


def fold_x(slab_array):
    inner_count = slab_array.shape[0] - 2
    from_high = passed_along(slab_array[0], "gx", -1)
    from_low = passed_along(slab_array[inner_count + 1], "gx", 1)
    interior = slab_array[1 : inner_count + 1]
    interior = interior.at[inner_count - 1].add(from_high)
    interior = interior.at[0].add(from_low)
    return interior


def fold_y(slab_array):
    inner_count = slab_array.shape[1] - 2
    from_high = passed_along(slab_array[:, 0], "gy", -1)
    from_low = passed_along(slab_array[:, inner_count + 1], "gy", 1)
    interior = slab_array[:, 1 : inner_count + 1]
    interior = interior.at[:, inner_count - 1].add(from_high)
    interior = interior.at[:, 0].add(from_low)
    return interior


def halving_scatter(block, axis):
    length = lax.axis_size(axis)
    index = lax.axis_index(axis)
    distance = length // 2
    while distance >= 1:
        half = block.shape[0] // 2
        lower, upper = block[:half], block[half:]
        upper_side = (index // distance) % 2 == 1
        keep = jnp.where(upper_side, upper, lower)
        send = jnp.where(upper_side, lower, upper)
        pairs = [(i, i ^ distance) for i in range(length)]
        block = keep + lax.ppermute(send, axis, pairs)
        distance //= 2
    return block


def swapped(x, axis):
    length = lax.axis_size(axis)
    return lax.ppermute(x, axis, [(i, i ^ 1) for i in range(length)])


def per_device(descriptors, derivatives, neighbours, valid, forces, pool, sparse_idx):
    tiles_x = descriptors.shape[1]
    tiles_y = descriptors.shape[2]
    tile_count = tiles_x * tiles_y
    slot_total = derivatives.shape[4]
    desc_width = descriptors.shape[4]
    sparse = pool[sparse_idx]
    sparse_count = sparse.shape[0]
    rows = 64 * slot_total
    ext_rows = (tiles_x + 2) * (tiles_y + 2) * 64

    flat_valid = valid.reshape(tile_count, 64)
    flat_desc = descriptors.reshape(tile_count, 64, desc_width)
    flat_desc = jnp.where(flat_valid[:, :, None] != 0, flat_desc, jnp.zeros_like(flat_desc))
    scores = lax.dot_general(
        flat_desc, sparse, (((2,), (1,)), ((), ())), preferred_element_type=jnp.float32
    )
    flat_deriv = derivatives.reshape(tile_count, rows, 3, desc_width)
    projected = lax.dot_general(
        flat_deriv, sparse, (((3,), (1,)), ((), ())), preferred_element_type=jnp.float32
    )
    scores_rep = jnp.repeat(scores, slot_total, axis=1)
    contribution = (-2.0 * scores_rep)[:, :, None, :] * projected
    high_wide = lax.reduce_precision(contribution, exponent_bits=8, mantissa_bits=7)
    high = high_wide.astype(jnp.bfloat16)
    low = (contribution - high_wide).astype(jnp.bfloat16)
    parts = jnp.concatenate([high, low], axis=0).reshape(2 * tile_count, rows, 3 * sparse_count)

    tile_ids = jnp.arange(tile_count, dtype=jnp.int32)
    tile_x = (tile_ids // tiles_y)[:, None]
    tile_y = (tile_ids % tiles_y)[:, None]
    flat_nbr = neighbours.reshape(tile_count, rows)
    slot_code = flat_nbr // 64
    target_atom = flat_nbr % 64
    ext_x = tile_x + slot_code // 3
    ext_y = tile_y + slot_code % 3
    target_tile = ext_x * (tiles_y + 2) + ext_y

    def gathered(tiles):
        lookup = np.full((tiles_x + 2) * (tiles_y + 2), -1, np.int32)
        for place, (x, y) in enumerate(tiles):
            lookup[x * (tiles_y + 2) + y] = place
        key = jnp.asarray(lookup)[target_tile] * 64 + target_atom
        onehot = (
            jnp.arange(len(tiles) * 64, dtype=jnp.int32)[None, :, None] == key[:, None, :]
        ).astype(jnp.bfloat16)
        onehot = jnp.concatenate([onehot, onehot], axis=0)
        summed = lax.dot_general(
            onehot, parts, (((0, 2), (0, 1)), ((), ())), preferred_element_type=jnp.float32
        )
        return summed.reshape(len(tiles), 64, 3, sparse_count)

    ext_cols = range(tiles_x + 2)
    edge_y = gathered([(x, 0) for x in ext_cols] + [(x, tiles_y + 1) for x in ext_cols])
    edge_y = edge_y.reshape(2, tiles_x + 2, 64, 3, sparse_count)
    from_high_y = passed_along(edge_y[0], "gy", -1)
    from_low_y = passed_along(edge_y[1], "gy", 1)
    inner_y = range(1, tiles_y + 1)
    edge_x = gathered([(0, y) for y in inner_y] + [(tiles_x + 1, y) for y in inner_y])
    edge_x = edge_x.reshape(2, tiles_y, 64, 3, sparse_count)
    own = gathered([(x, y) for x in range(1, tiles_x + 1) for y in inner_y])
    own = own.reshape(tiles_x, tiles_y, 64, 3, sparse_count)
    edge_x = edge_x.at[:, tiles_y - 1].add(from_high_y[:: tiles_x + 1])
    edge_x = edge_x.at[:, 0].add(from_low_y[:: tiles_x + 1])
    from_high_x = passed_along(edge_x[0], "gx", -1)
    from_low_x = passed_along(edge_x[1], "gx", 1)
    own = own.at[:, tiles_y - 1].add(from_high_y[1 : tiles_x + 1])
    own = own.at[:, 0].add(from_low_y[1 : tiles_x + 1])
    own = own.at[tiles_x - 1].add(from_high_x)
    own = own.at[0].add(from_low_x)
    design = own.astype(jnp.bfloat16)

    valid_own = valid[0]
    masked = design * valid_own[:, :, :, None, None].astype(jnp.bfloat16)
    masked_rows = masked.reshape(-1, sparse_count)
    force_own = forces[0].astype(jnp.float32)
    local_sumsq = jnp.sum(valid_own[:, :, :, None].astype(jnp.float32) * force_own * force_own)

    gx_size = lax.axis_size("gx")
    gy_size = lax.axis_size("gy")
    share = sparse_count // (gx_size * gy_size)
    pad_cols = 128
    reordered = masked_rows.reshape(-1, gx_size, gy_size, share).swapaxes(1, 2)
    reordered = reordered.reshape(-1, sparse_count)
    right = jnp.concatenate(
        [
            masked_rows,
            forces[0].reshape(-1, 1),
            jnp.zeros((masked_rows.shape[0], pad_cols - 1), jnp.bfloat16),
        ],
        axis=1,
    )
    packed = lax.dot_general(
        reordered, right, (((0,), (0,)), ((), ())), preferred_element_type=jnp.float32
    )
    packed = packed.at[:, sparse_count + 1].set(local_sumsq)
    reduced = lax.psum_scatter(packed, "gy", scatter_dimension=0, tiled=True)
    reduced = halving_scatter(reduced, "gx")
    weighted = reduced / reduced[:, sparse_count + 1 : sparse_count + 2]
    total = weighted + swapped(weighted, "cfg")
    gram = total[:, :sparse_count]
    rhs = total[:, sparse_count]
    return (design[None], gram, rhs)


def solution(mesh):
    in_specs = (
        P("cfg", "gx", "gy", None, None),
        P("cfg", "gx", "gy", None, None, None, None),
        P("cfg", "gx", "gy", None, None),
        P("cfg", "gx", "gy", None),
        P("cfg", "gx", "gy", None, None),
        P(),
        P(),
    )
    out_specs = (P("cfg", "gx", "gy", None, None, None), P(("gx", "gy"), None), P(("gx", "gy")))
    return jax.shard_map(
        per_device, mesh=mesh, in_specs=in_specs, out_specs=out_specs, check_vma=False
    )
```

```python
import jax
import jax.numpy as jnp
from jax import lax
from jax.sharding import PartitionSpec as P


def passed_along(x, axis, by):
    length = lax.axis_size(axis)
    return lax.ppermute(x, axis, [(i, (i + by) % length) for i in range(length)])


def fold_x(slab_array):
    inner_count = slab_array.shape[0] - 2
    from_high = passed_along(slab_array[0], "gx", -1)
    from_low = passed_along(slab_array[inner_count + 1], "gx", 1)
    interior = slab_array[1 : inner_count + 1]
    interior = interior.at[inner_count - 1].add(from_high)
    interior = interior.at[0].add(from_low)
    return interior


def fold_y(slab_array):
    inner_count = slab_array.shape[1] - 2
    from_high = passed_along(slab_array[:, 0], "gy", -1)
    from_low = passed_along(slab_array[:, inner_count + 1], "gy", 1)
    interior = slab_array[:, 1 : inner_count + 1]
    interior = interior.at[:, inner_count - 1].add(from_high)
    interior = interior.at[:, 0].add(from_low)
    return interior


def halving_scatter(block, axis):
    length = lax.axis_size(axis)
    index = lax.axis_index(axis)
    distance = length // 2
    while distance >= 1:
        half = block.shape[0] // 2
        lower, upper = block[:half], block[half:]
        upper_side = (index // distance) % 2 == 1
        keep = jnp.where(upper_side, upper, lower)
        send = jnp.where(upper_side, lower, upper)
        pairs = [(i, i ^ distance) for i in range(length)]
        block = keep + lax.ppermute(send, axis, pairs)
        distance //= 2
    return block


def swapped(x, axis):
    length = lax.axis_size(axis)
    return lax.ppermute(x, axis, [(i, i ^ 1) for i in range(length)])


def per_device(descriptors, derivatives, neighbours, valid, forces, pool, sparse_idx):
    tiles_x = descriptors.shape[1]
    tiles_y = descriptors.shape[2]
    tile_count = tiles_x * tiles_y
    slot_total = derivatives.shape[4]
    desc_width = descriptors.shape[4]
    sparse = pool[sparse_idx]
    sparse_count = sparse.shape[0]
    rows = 64 * slot_total
    ext_rows = (tiles_x + 2) * (tiles_y + 2) * 64

    flat_valid = valid.reshape(tile_count, 64)
    flat_desc = descriptors.reshape(tile_count, 64, desc_width)
    flat_desc = jnp.where(flat_valid[:, :, None] != 0, flat_desc, jnp.zeros_like(flat_desc))
    flat_deriv = derivatives.reshape(tile_count, rows, 3, desc_width)

    tile_ids = jnp.arange(tile_count, dtype=jnp.int32)
    tile_x = (tile_ids // tiles_y)[:, None]
    tile_y = (tile_ids % tiles_y)[:, None]
    flat_nbr = neighbours.reshape(tile_count, rows)
    slot_code = flat_nbr // 64
    target_atom = flat_nbr % 64
    ext_x = tile_x + slot_code // 3
    ext_y = tile_y + slot_code % 3
    target = (ext_x * (tiles_y + 2) + ext_y) * 64 + target_atom
    onehot = (
        jnp.arange(ext_rows, dtype=jnp.int32)[None, :, None] == target[:, None, :]
    ).astype(jnp.bfloat16)
    onehot = jnp.concatenate([onehot, onehot], axis=0)

    def owned_part(sparse_part):
        width = sparse_part.shape[0]
        scores = lax.dot_general(
            flat_desc, sparse_part, (((2,), (1,)), ((), ())), preferred_element_type=jnp.float32
        )
        projected = lax.dot_general(
            flat_deriv, sparse_part, (((3,), (1,)), ((), ())), preferred_element_type=jnp.float32
        )
        scores_rep = jnp.repeat(scores, slot_total, axis=1)
        contribution = (-2.0 * scores_rep)[:, :, None, :] * projected
        high_wide = lax.reduce_precision(contribution, exponent_bits=8, mantissa_bits=7)
        high = high_wide.astype(jnp.bfloat16)
        low = (contribution - high_wide).astype(jnp.bfloat16)
        parts = jnp.concatenate([high, low], axis=0).reshape(2 * tile_count, rows, 3 * width)
        accumulator = lax.dot_general(
            onehot, parts, (((0, 2), (0, 1)), ((), ())), preferred_element_type=jnp.float32
        )
        extended = accumulator.reshape(tiles_x + 2, tiles_y + 2, 64, 3, width)
        return fold_x(fold_y(extended))

    chunks = 2
    chunk_width = sparse_count // chunks
    owned = jnp.concatenate(
        [owned_part(sparse[c * chunk_width : (c + 1) * chunk_width]) for c in range(chunks)],
        axis=-1,
    )
    design = owned.astype(jnp.bfloat16)

    valid_own = valid[0]
    masked = design * valid_own[:, :, :, None, None].astype(jnp.bfloat16)
    masked_rows = masked.reshape(-1, sparse_count)
    force_own = forces[0].astype(jnp.float32)
    local_sumsq = jnp.sum(valid_own[:, :, :, None].astype(jnp.float32) * force_own * force_own)
    gram_part = lax.dot_general(
        masked_rows, masked_rows, (((0,), (0,)), ((), ())), preferred_element_type=jnp.float32
    )
    rhs_part = jnp.dot(forces[0].reshape(-1), masked_rows, preferred_element_type=jnp.float32)

    pad_cols = 128
    extra = jnp.zeros((sparse_count, pad_cols), jnp.float32)
    extra = extra.at[:, 0].set(rhs_part).at[:, 1].set(local_sumsq)
    packed = jnp.concatenate([gram_part, extra], axis=1)
    gx_size = lax.axis_size("gx")
    gy_size = lax.axis_size("gy")
    packed = packed.reshape(gx_size, gy_size, -1, packed.shape[1]).swapaxes(0, 1)
    packed = packed.reshape(sparse_count, -1)
    reduced = lax.psum_scatter(packed, "gy", scatter_dimension=0, tiled=True)
    reduced = halving_scatter(reduced, "gx")
    weighted = reduced / reduced[:, sparse_count + 1 : sparse_count + 2]
    total = weighted + swapped(weighted, "cfg")
    gram = total[:, :sparse_count]
    rhs = total[:, sparse_count]
    return (design[None], gram, rhs)


def solution(mesh):
    in_specs = (
        P("cfg", "gx", "gy", None, None),
        P("cfg", "gx", "gy", None, None, None, None),
        P("cfg", "gx", "gy", None, None),
        P("cfg", "gx", "gy", None),
        P("cfg", "gx", "gy", None, None),
        P(),
        P(),
    )
    out_specs = (P("cfg", "gx", "gy", None, None, None), P(("gx", "gy"), None), P(("gx", "gy")))
    return jax.shard_map(
        per_device, mesh=mesh, in_specs=in_specs, out_specs=out_specs, check_vma=False
    )
```

```python
import jax
import jax.numpy as jnp
from jax import lax
from jax.sharding import PartitionSpec as P


def passed_along(x, axis, by):
    length = lax.axis_size(axis)
    return lax.ppermute(x, axis, [(i, (i + by) % length) for i in range(length)])


def fold_x(slab_array):
    inner_count = slab_array.shape[0] - 2
    from_high = passed_along(slab_array[0], "gx", -1)
    from_low = passed_along(slab_array[inner_count + 1], "gx", 1)
    interior = slab_array[1 : inner_count + 1]
    interior = interior.at[inner_count - 1].add(from_high)
    interior = interior.at[0].add(from_low)
    return interior


def fold_y(slab_array):
    inner_count = slab_array.shape[1] - 2
    from_high = passed_along(slab_array[:, 0], "gy", -1)
    from_low = passed_along(slab_array[:, inner_count + 1], "gy", 1)
    interior = slab_array[:, 1 : inner_count + 1]
    interior = interior.at[:, inner_count - 1].add(from_high)
    interior = interior.at[:, 0].add(from_low)
    return interior


def halving_scatter(block, axis):
    length = lax.axis_size(axis)
    index = lax.axis_index(axis)
    distance = length // 2
    while distance >= 1:
        half = block.shape[0] // 2
        lower, upper = block[:half], block[half:]
        upper_side = (index // distance) % 2 == 1
        keep = jnp.where(upper_side, upper, lower)
        send = jnp.where(upper_side, lower, upper)
        pairs = [(i, i ^ distance) for i in range(length)]
        block = keep + lax.ppermute(send, axis, pairs)
        distance //= 2
    return block


def swapped(x, axis):
    length = lax.axis_size(axis)
    return lax.ppermute(x, axis, [(i, i ^ 1) for i in range(length)])


def per_device(descriptors, derivatives, neighbours, valid, forces, pool, sparse_idx):
    tiles_x = descriptors.shape[1]
    tiles_y = descriptors.shape[2]
    tile_count = tiles_x * tiles_y
    slot_total = derivatives.shape[4]
    desc_width = descriptors.shape[4]
    sparse = pool[sparse_idx]
    sparse_count = sparse.shape[0]
    rows = 64 * slot_total
    ext_rows = (tiles_x + 2) * (tiles_y + 2) * 64

    flat_valid = valid.reshape(tile_count, 64)
    flat_desc = descriptors.reshape(tile_count, 64, desc_width)
    flat_desc = jnp.where(flat_valid[:, :, None] != 0, flat_desc, jnp.zeros_like(flat_desc))
    flat_deriv = derivatives.reshape(tile_count, rows, 3, desc_width)

    tile_ids = jnp.arange(tile_count, dtype=jnp.int32)
    tile_x = (tile_ids // tiles_y)[:, None]
    tile_y = (tile_ids % tiles_y)[:, None]
    flat_nbr = neighbours.reshape(tile_count, rows)
    slot_code = flat_nbr // 64
    target_atom = flat_nbr % 64
    ext_x = tile_x + slot_code // 3
    ext_y = tile_y + slot_code % 3
    target = (ext_x * (tiles_y + 2) + ext_y) * 64 + target_atom
    onehot = (
        jnp.arange(ext_rows, dtype=jnp.int32)[None, :, None] == target[:, None, :]
    ).astype(jnp.bfloat16)
    onehot = jnp.concatenate([onehot, onehot], axis=0)

    def owned_part(sparse_part):
        width = sparse_part.shape[0]
        scores = lax.dot_general(
            flat_desc, sparse_part, (((2,), (1,)), ((), ())), preferred_element_type=jnp.float32
        )
        projected = lax.dot_general(
            flat_deriv, sparse_part, (((3,), (1,)), ((), ())), preferred_element_type=jnp.float32
        )
        scores_rep = jnp.repeat(scores, slot_total, axis=1)
        contribution = (-2.0 * scores_rep)[:, :, None, :] * projected
        high_wide = lax.reduce_precision(contribution, exponent_bits=8, mantissa_bits=7)
        high = high_wide.astype(jnp.bfloat16)
        low = (contribution - high_wide).astype(jnp.bfloat16)
        parts = jnp.concatenate([high, low], axis=0).reshape(2 * tile_count, rows, 3 * width)
        accumulator = lax.dot_general(
            onehot, parts, (((0, 2), (0, 1)), ((), ())), preferred_element_type=jnp.float32
        )
        extended = accumulator.reshape(tiles_x + 2, tiles_y + 2, 64, 3, width)
        return fold_x(fold_y(extended))

    chunks = 4
    chunk_width = sparse_count // chunks
    owned = jnp.concatenate(
        [owned_part(sparse[c * chunk_width : (c + 1) * chunk_width]) for c in range(chunks)],
        axis=-1,
    )
    design = owned.astype(jnp.bfloat16)

    valid_own = valid[0]
    masked = design * valid_own[:, :, :, None, None].astype(jnp.bfloat16)
    masked_rows = masked.reshape(-1, sparse_count)
    force_own = forces[0].astype(jnp.float32)
    local_sumsq = jnp.sum(valid_own[:, :, :, None].astype(jnp.float32) * force_own * force_own)
    gram_part = lax.dot_general(
        masked_rows, masked_rows, (((0,), (0,)), ((), ())), preferred_element_type=jnp.float32
    )
    rhs_part = jnp.dot(forces[0].reshape(-1), masked_rows, preferred_element_type=jnp.float32)

    pad_cols = 128
    gx_size = lax.axis_size("gx")
    gy_size = lax.axis_size("gy")
    extra = jnp.zeros((sparse_count, pad_cols), jnp.float32)
    extra = extra.at[:, 0].set(rhs_part).at[:, 1].set(local_sumsq)

    def reordered(x):
        x = x.reshape(gx_size, gy_size, -1, x.shape[1]).swapaxes(0, 1)
        return x.reshape(sparse_count, -1)

    packed = jnp.concatenate([reordered(gram_part), reordered(extra)], axis=1)
    reduced = lax.psum_scatter(packed, "gy", scatter_dimension=0, tiled=True)
    reduced = halving_scatter(reduced, "gx")
    weighted = reduced / reduced[:, sparse_count + 1 : sparse_count + 2]
    total = weighted + swapped(weighted, "cfg")
    gram = total[:, :sparse_count]
    rhs = total[:, sparse_count]
    return (design[None], gram, rhs)


def solution(mesh):
    in_specs = (
        P("cfg", "gx", "gy", None, None),
        P("cfg", "gx", "gy", None, None, None, None),
        P("cfg", "gx", "gy", None, None),
        P("cfg", "gx", "gy", None),
        P("cfg", "gx", "gy", None, None),
        P(),
        P(),
    )
    out_specs = (P("cfg", "gx", "gy", None, None, None), P(("gx", "gy"), None), P(("gx", "gy")))
    return jax.shard_map(
        per_device, mesh=mesh, in_specs=in_specs, out_specs=out_specs, check_vma=False
    )
```

```python
import jax
import jax.numpy as jnp
from jax import lax
from jax.sharding import PartitionSpec as P

CHUNKS = 4


def passed_along(x, axis, by):
    length = lax.axis_size(axis)
    return lax.ppermute(x, axis, [(i, (i + by) % length) for i in range(length)])


def fold_x(slab_array):
  inner_count = slab_array.shape[0] - 2
  from_high = passed_along(slab_array[0], "gx", -1)
  from_low = passed_along(slab_array[inner_count + 1], "gx", 1)
  interior = slab_array[1 : inner_count + 1]
  interior = interior.at[inner_count - 1].add(from_high)
  interior = interior.at[0].add(from_low)
  return interior


def fold_y(slab_array):
  inner_count = slab_array.shape[1] - 2
  from_high = passed_along(slab_array[:, 0], "gy", -1)
  from_low = passed_along(slab_array[:, inner_count + 1], "gy", 1)
  interior = slab_array[:, 1 : inner_count + 1]
  interior = interior.at[:, inner_count - 1].add(from_high)
  interior = interior.at[:, 0].add(from_low)
  return interior


def halving_scatter(block, axis):
    length = lax.axis_size(axis)
    index = lax.axis_index(axis)
    distance = length // 2
    while distance >= 1:
        half = block.shape[0] // 2
        lower, upper = block[:half], block[half:]
        upper_side = (index // distance) % 2 == 1
        keep = jnp.where(upper_side, upper, lower)
        send = jnp.where(upper_side, lower, upper)
        pairs = [(i, i ^ distance) for i in range(length)]
        block = keep + lax.ppermute(send, axis, pairs)
        distance //= 2
    return block


def swapped(x, axis):
    length = lax.axis_size(axis)
    return lax.ppermute(x, axis, [(i, i ^ 1) for i in range(length)])


def per_device(descriptors, derivatives, neighbours, valid, forces, pool, sparse_idx):
    tiles_x = descriptors.shape[1]
    tiles_y = descriptors.shape[2]
    tile_count = tiles_x * tiles_y
    slot_total = derivatives.shape[4]
    desc_width = descriptors.shape[4]
    sparse = pool[sparse_idx]
    sparse_count = sparse.shape[0]
    rows = 64 * slot_total
    ext_rows = (tiles_x + 2) * (tiles_y + 2) * 64

    flat_valid = valid.reshape(tile_count, 64)
    flat_desc = descriptors.reshape(tile_count, 64, desc_width)
    flat_desc = jnp.where(flat_valid[:, :, None] != 0, flat_desc, jnp.zeros_like(flat_desc))
    flat_deriv = derivatives.reshape(tile_count, rows, 3, desc_width)

    tile_ids = jnp.arange(tile_count, dtype=jnp.int32)
    tile_x = (tile_ids // tiles_y)[:, None]
    tile_y = (tile_ids % tiles_y)[:, None]
    flat_nbr = neighbours.reshape(tile_count, rows)
    slot_code = flat_nbr // 64
    target_atom = flat_nbr % 64
    ext_x = tile_x + slot_code // 3
    ext_y = tile_y + slot_code % 3
    target = (ext_x * (tiles_y + 2) + ext_y) * 64 + target_atom
    onehot = (
        jnp.arange(ext_rows, dtype=jnp.int32)[None, :, None] == target[:, None, :]
    ).astype(jnp.bfloat16)
    onehot = jnp.concatenate([onehot, onehot], axis=0)

    def owned_part(sparse_part):
        return fold_x(fold_y(worked(sparse_part)))

    def worked(sparse_part):
        width = sparse_part.shape[0]
        scores = lax.dot_general(
            flat_desc, sparse_part, (((2,), (1,)), ((), ())), preferred_element_type=jnp.float32
        )
        projected = lax.dot_general(
            flat_deriv, sparse_part, (((3,), (1,)), ((), ())), preferred_element_type=jnp.float32
        )
        scores_rep = jnp.repeat(scores, slot_total, axis=1)
        contribution = (-2.0 * scores_rep)[:, :, None, :] * projected
        high_wide = lax.reduce_precision(contribution, exponent_bits=8, mantissa_bits=7)
        high = high_wide.astype(jnp.bfloat16)
        low = (contribution - high_wide).astype(jnp.bfloat16)
        parts = jnp.concatenate([high, low], axis=0).reshape(2 * tile_count, rows, 3 * width)
        accumulator = lax.dot_general(
            onehot, parts, (((0, 2), (0, 1)), ((), ())), preferred_element_type=jnp.float32
        )
        return accumulator.reshape(tiles_x + 2, tiles_y + 2, 64, 3, width)

    chunks = CHUNKS
    chunk_width = sparse_count // chunks
    pieces = []
    for c in range(chunks):
        pieces.append(owned_part(sparse[c * chunk_width : (c + 1) * chunk_width]))
    owned = jnp.concatenate(pieces, axis=-1)
    design = owned.astype(jnp.bfloat16)

    valid_own = valid[0]
    masked = design * valid_own[:, :, :, None, None].astype(jnp.bfloat16)
    masked_rows = masked.reshape(-1, sparse_count)
    force_own = forces[0].astype(jnp.float32)
    local_sumsq = jnp.sum(valid_own[:, :, :, None].astype(jnp.float32) * force_own * force_own)
    gram_part = lax.dot_general(
        masked_rows, masked_rows, (((0,), (0,)), ((), ())), preferred_element_type=jnp.float32
    )
    rhs_part = jnp.dot(forces[0].reshape(-1), masked_rows, preferred_element_type=jnp.float32)

    pad_cols = 128
    gx_size = lax.axis_size("gx")
    gy_size = lax.axis_size("gy")
    extra = jnp.zeros((sparse_count, pad_cols), jnp.float32)
    extra = extra.at[:, 0].set(rhs_part).at[:, 1].set(local_sumsq)

    def reordered(x):
        x = x.reshape(gx_size, gy_size, -1, x.shape[1]).swapaxes(0, 1)
        return x.reshape(sparse_count, -1)

    packed = jnp.concatenate([reordered(gram_part), reordered(extra)], axis=1)
    reduced = lax.psum_scatter(packed, "gy", scatter_dimension=0, tiled=True)
    reduced = halving_scatter(reduced, "gx")
    weighted = reduced / reduced[:, sparse_count + 1 : sparse_count + 2]
    total = weighted + swapped(weighted, "cfg")
    gram = total[:, :sparse_count]
    rhs = total[:, sparse_count]
    return (design[None], gram, rhs)


def solution(mesh):
    in_specs = (
        P("cfg", "gx", "gy", None, None),
        P("cfg", "gx", "gy", None, None, None, None),
        P("cfg", "gx", "gy", None, None),
        P("cfg", "gx", "gy", None),
        P("cfg", "gx", "gy", None, None),
        P(),
        P(),
    )
    out_specs = (P("cfg", "gx", "gy", None, None, None), P(("gx", "gy"), None), P(("gx", "gy")))

    return jax.shard_map(
        per_device, mesh=mesh, in_specs=in_specs, out_specs=out_specs, check_vma=False
    )
```

```python
import jax
import jax.numpy as jnp
from jax import lax
from jax.sharding import PartitionSpec as P

CHUNKS = 4


def passed_along(x, axis, by):
    length = lax.axis_size(axis)
    return lax.ppermute(x, axis, [(i, (i + by) % length) for i in range(length)])


def fold_x(slab_array):
  inner_count = slab_array.shape[0] - 2
  from_high = passed_along(slab_array[0], "gx", -1)
  from_low = passed_along(slab_array[inner_count + 1], "gx", 1)
  interior = slab_array[1 : inner_count + 1]
  interior = interior.at[inner_count - 1].add(from_high)
  interior = interior.at[0].add(from_low)
  return interior


def fold_y(slab_array):
  inner_count = slab_array.shape[1] - 2
  from_high = passed_along(slab_array[:, 0], "gy", -1)
  from_low = passed_along(slab_array[:, inner_count + 1], "gy", 1)
  interior = slab_array[:, 1 : inner_count + 1]
  interior = interior.at[:, inner_count - 1].add(from_high)
  interior = interior.at[:, 0].add(from_low)
  return interior


def halving_scatter(block, axis):
    length = lax.axis_size(axis)
    index = lax.axis_index(axis)
    distance = length // 2
    while distance >= 1:
        half = block.shape[0] // 2
        lower, upper = block[:half], block[half:]
        upper_side = (index // distance) % 2 == 1
        keep = jnp.where(upper_side, upper, lower)
        send = jnp.where(upper_side, lower, upper)
        pairs = [(i, i ^ distance) for i in range(length)]
        block = keep + lax.ppermute(send, axis, pairs)
        distance //= 2
    return block


def swapped(x, axis):
    length = lax.axis_size(axis)
    return lax.ppermute(x, axis, [(i, i ^ 1) for i in range(length)])


def per_device(descriptors, derivatives, neighbours, valid, forces, pool, sparse_idx):
    tiles_x = descriptors.shape[1]
    tiles_y = descriptors.shape[2]
    tile_count = tiles_x * tiles_y
    slot_total = derivatives.shape[4]
    desc_width = descriptors.shape[4]
    sparse = pool[sparse_idx]
    sparse_count = sparse.shape[0]
    rows = 64 * slot_total
    ext_rows = (tiles_x + 2) * (tiles_y + 2) * 64

    flat_valid = valid.reshape(tile_count, 64)
    flat_desc = descriptors.reshape(tile_count, 64, desc_width)
    flat_desc = jnp.where(flat_valid[:, :, None] != 0, flat_desc, jnp.zeros_like(flat_desc))
    flat_deriv = derivatives.reshape(tile_count, rows, 3, desc_width)

    tile_ids = jnp.arange(tile_count, dtype=jnp.int32)
    tile_x = (tile_ids // tiles_y)[:, None]
    tile_y = (tile_ids % tiles_y)[:, None]
    flat_nbr = neighbours.reshape(tile_count, rows)
    slot_code = flat_nbr // 64
    target_atom = flat_nbr % 64
    ext_x = tile_x + slot_code // 3
    ext_y = tile_y + slot_code % 3
    target = (ext_x * (tiles_y + 2) + ext_y) * 64 + target_atom
    onehot = (
        jnp.arange(ext_rows, dtype=jnp.int32)[None, :, None] == target[:, None, :]
    ).astype(jnp.bfloat16)
    onehot = jnp.concatenate([onehot, onehot], axis=0)

    def owned_part(sparse_part):
        return fold_x(fold_y(worked(sparse_part)))

    def worked(sparse_part):
        width = sparse_part.shape[0]
        scores = lax.dot_general(
            flat_desc, sparse_part, (((2,), (1,)), ((), ())), preferred_element_type=jnp.float32
        )
        projected = lax.dot_general(
            flat_deriv, sparse_part, (((3,), (1,)), ((), ())), preferred_element_type=jnp.float32
        )
        scores_rep = jnp.repeat(scores, slot_total, axis=1)
        contribution = (-2.0 * scores_rep)[:, :, None, :] * projected
        high_wide = lax.reduce_precision(contribution, exponent_bits=8, mantissa_bits=7)
        high = high_wide.astype(jnp.bfloat16)
        low = (contribution - high_wide).astype(jnp.bfloat16)
        parts = jnp.concatenate([high, low], axis=0).reshape(2 * tile_count, rows, 3 * width)
        accumulator = lax.dot_general(
            onehot, parts, (((0, 2), (0, 1)), ((), ())), preferred_element_type=jnp.float32
        )
        return accumulator.reshape(tiles_x + 2, tiles_y + 2, 64, 3, width)

    chunks = CHUNKS
    chunk_width = sparse_count // chunks
    pieces = []
    for c in range(chunks):
        pieces.append(owned_part(sparse[c * chunk_width : (c + 1) * chunk_width]))
    owned = jnp.concatenate(pieces, axis=-1)
    design = owned.astype(jnp.bfloat16)

    valid_own = valid[0]
    masked = design * valid_own[:, :, :, None, None].astype(jnp.bfloat16)
    masked_rows = masked.reshape(-1, sparse_count)
    force_own = forces[0].astype(jnp.float32)
    local_sumsq = jnp.sum(valid_own[:, :, :, None].astype(jnp.float32) * force_own * force_own)
    gram_part = lax.dot_general(
        masked_rows, masked_rows, (((0,), (0,)), ((), ())), preferred_element_type=jnp.float32
    )
    rhs_part = jnp.dot(forces[0].reshape(-1), masked_rows, preferred_element_type=jnp.float32)

    pad_cols = 128
    gx_size = lax.axis_size("gx")
    gy_size = lax.axis_size("gy")
    extra = jnp.zeros((sparse_count, pad_cols), jnp.float32)
    extra = extra.at[:, 0].set(rhs_part).at[:, 1].set(local_sumsq)

    def reordered(x):
        x = x.reshape(gx_size, gy_size, -1, x.shape[1]).swapaxes(0, 1)
        return x.reshape(sparse_count, -1)

    split = sparse_count - 3 * pad_cols
    first = reordered(gram_part[:, :split])
    first = lax.psum_scatter(first, "gy", scatter_dimension=0, tiled=True)
    first = halving_scatter(first, "gx")
    second = jnp.concatenate([gram_part[:, split:], extra], axis=1)
    second = halving_scatter(halving_scatter(second, "gx"), "gy")
    reduced = jnp.concatenate([first, second], axis=1)
    weighted = reduced / reduced[:, sparse_count + 1 : sparse_count + 2]
    total = weighted + swapped(weighted, "cfg")
    gram = total[:, :sparse_count]
    rhs = total[:, sparse_count]
    return (design[None], gram, rhs)


def solution(mesh):
    in_specs = (
        P("cfg", "gx", "gy", None, None),
        P("cfg", "gx", "gy", None, None, None, None),
        P("cfg", "gx", "gy", None, None),
        P("cfg", "gx", "gy", None),
        P("cfg", "gx", "gy", None, None),
        P(),
        P(),
    )
    out_specs = (P("cfg", "gx", "gy", None, None, None), P(("gx", "gy"), None), P(("gx", "gy")))

    return jax.shard_map(
        per_device, mesh=mesh, in_specs=in_specs, out_specs=out_specs, check_vma=False
    )
```
